256 devices in a mesh: seq: 64 (over y_hi, x, z), chan: 4 (over y_lo, core).
Axes of the slice: x: 4, y: 4 (y_hi: 2, y_lo: 2; y = y_hi * 2 + y_lo), z: 8, core: 2. Of those that a mesh axis runs over, the one named last changes fastest.
Arguments:
- value_in: bfloat16 [24576, 4096], P('seq', 'chan'), may hold values from -6 to 6
- gate_in: bfloat16 [24576, 4096], P('seq', 'chan'), may hold values from -6 to 6
- gate_out: bfloat16 [24576, 4096], P('seq', 'chan'), may hold values from -6 to 6
- spectral_filter: bfloat16 [24576, 4096], P('seq', 'chan'), may hold values from -6 to 6
- analysis_blocks: bfloat16 [3, 128, 128], replicated, may hold values from -0.5 to 0.5
- analysis_mix: bfloat16 [128, 3, 3], replicated, may hold values from -3.5 to 3.5
- synthesis_blocks: bfloat16 [3, 128, 128], replicated, may hold values from -0.5 to 0.5
- synthesis_mix: bfloat16 [128, 3, 3], replicated, may hold values from -3.5 to 3.5
- angles: float32 [6, 384], replicated, may hold values from -3.140625 to 3.140625
- out_weight: bfloat16 [4096, 4096], P('chan'), may hold values from -0.09375 to 0.09375
Outputs:
- projected: bfloat16 [24576, 4096], P(('seq', 'chan'))
The draws below stay inside these ranges and needn't reach their ends.
All inputs are finite; a program needn't handle non-finite values.
Results may differ from the reference program's by a relative error of at most 0.02.
Values may be sent and summed in bfloat16 or wider, within the bound.
No kernel may reach another device: no remote copies, remote signals or barrier semaphores. Data moves between devices by JAX's collectives and lax.ppermute only.
A program may use at most 64 MiB of HBM per device.

```python
import jax
import jax.numpy as jnp
from jax import lax

WIDTH = 4096
BLOCK = 128
TOK_DEV = 384
NB = 3
SECTIONS = 6
LENGTH = 24576
N_SEQ = 64


def block_levels(rng, shape, cuts, low, high):
    factor_of, own = 1.0, jax.random.fold_in(rng, 6)
    for axis_at, blocks in cuts:
        heights = jnp.exp(jax.random.uniform(jax.random.fold_in(own, axis_at), (blocks,), jnp.float32, low / len(cuts), high / len(cuts)))
        factor_of = factor_of * jnp.repeat(heights, shape[axis_at] // blocks).reshape([-1 if axis == axis_at else 1 for axis in range(len(shape))])
    return factor_of


def scatter_about(own_key, extent, scale, limit, split=(), held_as=jnp.bfloat16):
    loudness = block_levels(own_key, extent, split, -0.22, 0.18) if split else 1.0
    values = jax.random.normal(own_key, extent, jnp.float32) * scale * loudness
    return jnp.minimum(jnp.maximum(values, -limit), limit).astype(held_as)


def setup_inputs(seed: int = 0) -> dict:
    arg_keys = jax.random.split(jax.random.key(seed), 11)
    return {
        "value_in": scatter_about(arg_keys[0], (LENGTH, WIDTH), 1.0, 6.0, ((0, 64), (1, 4))),
        "gate_in": scatter_about(arg_keys[1], (LENGTH, WIDTH), 1.0, 6.0, ((0, 64), (1, 4))),
        "gate_out": scatter_about(arg_keys[2], (LENGTH, WIDTH), 1.0, 6.0, ((0, 64), (1, 4))),
        "spectral_filter": scatter_about(arg_keys[3], (LENGTH, WIDTH), 1.0, 6.0, ((0, 64), (1, 4))),
        "analysis_blocks": scatter_about(arg_keys[4], (NB, BLOCK, BLOCK), BLOCK ** -0.5, 0.5),
        "analysis_mix": scatter_about(arg_keys[5], (BLOCK, NB, NB), NB ** -0.5, 3.5),
        "synthesis_blocks": scatter_about(arg_keys[6], (NB, BLOCK, BLOCK), BLOCK ** -0.5, 0.5),
        "synthesis_mix": scatter_about(arg_keys[7], (BLOCK, NB, NB), NB ** -0.5, 3.5),
        "angles": jnp.clip(jax.random.uniform(arg_keys[8], (SECTIONS, TOK_DEV), jnp.float32, -3.140625, 3.140625), -3.140625, 3.140625),
        "out_weight": scatter_about(arg_keys[9], (WIDTH, WIDTH), WIDTH ** -0.5, 0.09375, ((0, 4),)),
    }


def rotate_section(values, theta, width, flip):
    count = values.shape[0]
    shaped = values.reshape((count // (2 * width), 2, width) + values.shape[1:]).astype(jnp.float32)
    cosine = jnp.cos(theta)[:, :, None]
    sine = flip * jnp.sin(theta)[:, :, None]
    lower = shaped[:, 0]
    upper = shaped[:, 1]
    new_lower = cosine * lower + sine * upper
    new_upper = cosine * upper - sine * lower
    return jnp.stack([new_lower, new_upper], axis=1).reshape(values.shape).astype(jnp.bfloat16)


def reference(value_in, gate_in, gate_out, spectral_filter, analysis_blocks, analysis_mix, synthesis_blocks, synthesis_mix, angles, out_weight):
    grid = (N_SEQ, NB, BLOCK, WIDTH)
    mixed = (gate_in.astype(jnp.float32) * value_in.astype(jnp.float32)).astype(jnp.bfloat16).reshape(grid)
    inner = jnp.einsum('kij,nkjc->nkic', analysis_blocks.astype(jnp.float32), mixed.astype(jnp.float32)).astype(jnp.bfloat16)
    inner = lax.optimization_barrier(inner)
    spec = jnp.einsum('ikl,nlic->nkic', analysis_mix.astype(jnp.float32), inner.astype(jnp.float32)).astype(jnp.bfloat16)
    theta = angles.reshape(SECTIONS, NB, BLOCK)
    for section in range(SECTIONS):
        spec = rotate_section(spec, theta[section], 2 ** section, 1.0)
    spec = (spec.astype(jnp.float32) * spectral_filter.reshape(grid).astype(jnp.float32)).astype(jnp.bfloat16)
    for section in reversed(range(SECTIONS)):
        spec = rotate_section(spec, theta[section], 2 ** section, -1.0)
    spread = jnp.einsum('ikl,nlic->nkic', synthesis_mix.astype(jnp.float32), spec.astype(jnp.float32)).astype(jnp.bfloat16)
    spread = lax.optimization_barrier(spread)
    conv = jnp.einsum('kij,nkjc->nkic', synthesis_blocks.astype(jnp.float32), spread.astype(jnp.float32))
    gated = (gate_out.astype(jnp.float32) * conv.reshape(N_SEQ * NB * BLOCK, WIDTH)).astype(jnp.bfloat16)
    return jnp.dot(gated, out_weight, preferred_element_type=jnp.float32).astype(jnp.bfloat16)
```

```python
import jax
import jax.numpy as jnp
from jax import lax
from jax.sharding import PartitionSpec as P

ROW_SPLIT = 8


def to_columns(values, count):
    nb, blk, chans = values.shape
    cs = count // ROW_SPLIT
    parts = values.reshape(nb, ROW_SPLIT, blk // ROW_SPLIT, cs, chans // cs)
    parts = parts.transpose(1, 3, 0, 2, 4).reshape(count, nb, blk // ROW_SPLIT, chans // cs)
    return lax.all_to_all(parts, "seq", 0, 0, tiled=True)


def from_columns(values, count, blk, chans):
    nb = values.shape[1]
    cs = count // ROW_SPLIT
    back = lax.all_to_all(values, "seq", 0, 0, tiled=True)
    back = back.reshape(ROW_SPLIT, cs, nb, blk // ROW_SPLIT, chans // cs)
    return back.transpose(2, 0, 3, 1, 4).reshape(nb, blk, chans)


def rotate_bit(values, cosine, sine, bit, sections, sign):
    axis = sections - 1 - bit
    lower = lax.index_in_dim(values, 0, axis, keepdims=True)
    upper = lax.index_in_dim(values, 1, axis, keepdims=True)
    new_lower = cosine * lower + sign * sine * upper
    new_upper = cosine * upper - sign * sine * lower
    return jnp.concatenate([new_lower, new_upper], axis=axis)


def per_device(
    value_in,
    gate_in,
    gate_out,
    spectral_filter,
    analysis_blocks,
    analysis_mix,
    synthesis_blocks,
    synthesis_mix,
    angles,
    out_weight,
):
    tokens, chans = value_in.shape
    nblocks = analysis_blocks.shape[0]
    blk = analysis_blocks.shape[1]
    count = lax.axis_size("seq")
    sections = count.bit_length() - 1
    rank = lax.axis_index("seq")
    mixed = (
        (gate_in.astype(jnp.float32) * value_in.astype(jnp.float32))
        .astype(jnp.bfloat16)
        .reshape(nblocks, blk, chans)
    )
    inner = jnp.einsum(
        "kij,kjc->kic", analysis_blocks, mixed, preferred_element_type=jnp.float32
    ).astype(jnp.bfloat16)
    spec = jnp.einsum(
        "ikl,lic->kic", analysis_mix, inner, preferred_element_type=jnp.float32
    ).astype(jnp.bfloat16)

    spec_cols = to_columns(spec, count)
    filt_cols = to_columns(spectral_filter.reshape(nblocks, blk, chans), count)
    rows = blk // ROW_SPLIT
    row_part = rank // (count // ROW_SPLIT)
    theta = angles.reshape(sections, nblocks, ROW_SPLIT, rows)
    theta = lax.dynamic_index_in_dim(theta, row_part, axis=2, keepdims=False)
    cosines = jnp.cos(theta)[:, :, :, None]
    sines = jnp.sin(theta)[:, :, :, None]

    shape = (2,) * sections + spec_cols.shape[1:]
    work = spec_cols.astype(jnp.float32).reshape(shape)
    for section in range(sections):
        work = rotate_bit(work, cosines[section], sines[section], section, sections, 1.0)
    work = work * filt_cols.astype(jnp.float32).reshape(shape)
    for section in reversed(range(sections)):
        work = rotate_bit(work, cosines[section], sines[section], section, sections, -1.0)
    work = work.astype(jnp.bfloat16).reshape(spec_cols.shape)

    grid = from_columns(work, count, blk, chans)
    spread = jnp.einsum(
        "ikl,lic->kic", synthesis_mix, grid, preferred_element_type=jnp.float32
    ).astype(jnp.bfloat16)
    conv = jnp.einsum("kij,kjc->kic", synthesis_blocks, spread, preferred_element_type=jnp.float32)
    gated = (gate_out.astype(jnp.float32) * conv.reshape(tokens, chans)).astype(jnp.bfloat16)
    return lax.psum_scatter(
        jnp.dot(gated, out_weight, preferred_element_type=jnp.float32).astype(jnp.bfloat16),
        "chan",
        scatter_dimension=0,
        tiled=True,
    )


def solution(mesh):
    placed = (
        P("seq", "chan"),
        P("seq", "chan"),
        P("seq", "chan"),
        P("seq", "chan"),
        P(),
        P(),
        P(),
        P(),
        P(),
        P("chan", None),
    )
    return jax.shard_map(
        per_device, mesh=mesh, in_specs=placed, out_specs=P(("seq", "chan"), None), check_vma=False
    )
```

```python
import jax
import jax.numpy as jnp
from jax import lax
from jax.sharding import PartitionSpec as P

ROW_SPLIT = 8


def to_columns(values, count):
    nb, blk, chans = values.shape
    cs = count // ROW_SPLIT
    parts = values.reshape(nb, ROW_SPLIT, blk // ROW_SPLIT, cs, chans // cs)
    parts = parts.transpose(1, 3, 0, 2, 4).reshape(count, nb, blk // ROW_SPLIT, chans // cs)
    return lax.all_to_all(parts, "seq", 0, 0, tiled=True)


def from_columns(values, count, blk, chans):
    nb = values.shape[1]
    cs = count // ROW_SPLIT
    back = lax.all_to_all(values, "seq", 0, 0, tiled=True)
    back = back.reshape(ROW_SPLIT, cs, nb, blk // ROW_SPLIT, chans // cs)
    return back.transpose(2, 0, 3, 1, 4).reshape(nb, blk, chans)


def rotate_bit(values, cosine, sine, bit, sections, sign):
    axis = sections - 1 - bit
    lower = lax.index_in_dim(values, 0, axis, keepdims=True)
    upper = lax.index_in_dim(values, 1, axis, keepdims=True)
    new_lower = cosine * lower + sign * sine * upper
    new_upper = cosine * upper - sign * sine * lower
    return jnp.concatenate([new_lower, new_upper], axis=axis)


def per_device(
    value_in,
    gate_in,
    gate_out,
    spectral_filter,
    analysis_blocks,
    analysis_mix,
    synthesis_blocks,
    synthesis_mix,
    angles,
    out_weight,
):
    tokens, chans = value_in.shape
    nblocks = analysis_blocks.shape[0]
    blk = analysis_blocks.shape[1]
    count = lax.axis_size("seq")
    sections = count.bit_length() - 1
    rank = lax.axis_index("seq")
    mixed = (
        (gate_in.astype(jnp.float32) * value_in.astype(jnp.float32))
        .astype(jnp.bfloat16)
        .reshape(nblocks, blk, chans)
    )
    inner = jnp.einsum(
        "kij,kjc->kic", analysis_blocks, mixed, preferred_element_type=jnp.float32
    ).astype(jnp.bfloat16)
    spec = jnp.einsum(
        "ikl,lic->kic", analysis_mix, inner, preferred_element_type=jnp.float32
    ).astype(jnp.bfloat16)

    spec_cols = to_columns(spec, count)
    filt_cols = to_columns(spectral_filter.reshape(nblocks, blk, chans), count)
    rows = blk // ROW_SPLIT
    row_part = rank // (count // ROW_SPLIT)
    theta = angles.reshape(sections, nblocks, ROW_SPLIT, rows)
    theta = lax.dynamic_index_in_dim(theta, row_part, axis=2, keepdims=False)
    cosines = jnp.cos(theta)[:, :, :, None]
    sines = jnp.sin(theta)[:, :, :, None]

    shape = (2,) * sections + spec_cols.shape[1:]
    work = spec_cols.astype(jnp.float32).reshape(shape)
    for section in range(sections):
        work = rotate_bit(work, cosines[section], sines[section], section, sections, 1.0)
    work = work * filt_cols.astype(jnp.float32).reshape(shape)
    for section in reversed(range(sections)):
        work = rotate_bit(work, cosines[section], sines[section], section, sections, -1.0)
    work = work.astype(jnp.bfloat16).reshape(spec_cols.shape)

    grid = from_columns(work, count, blk, chans)
    spread = jnp.einsum(
        "ikl,lic->kic", synthesis_mix, grid, preferred_element_type=jnp.float32
    ).astype(jnp.bfloat16)
    conv = jnp.einsum("kij,kjc->kic", synthesis_blocks, spread, preferred_element_type=jnp.float32)
    gated = (gate_out.astype(jnp.float32) * conv.reshape(tokens, chans)).astype(jnp.bfloat16)
    product = jnp.dot(gated, out_weight, preferred_element_type=jnp.float32)
    return scatter_sum(product)


def exchange(value, distance):
    pairs = [(source, source ^ distance) for source in range(lax.axis_size("chan"))]
    return lax.ppermute(value, "chan", pairs)


def scatter_sum(product):
    me = lax.axis_index("chan")
    core = me % 2
    chip = me // 2
    rows, width = product.shape
    quarters = product.reshape(2, 2, rows // 4, width)
    keep = lax.dynamic_index_in_dim(quarters, core, axis=1, keepdims=False)
    send = lax.dynamic_index_in_dim(quarters, 1 - core, axis=1, keepdims=False)
    half = keep + exchange(send.astype(jnp.bfloat16), 1).astype(jnp.float32)
    keep = lax.dynamic_index_in_dim(half, chip, axis=0, keepdims=False)
    send = lax.dynamic_index_in_dim(half, 1 - chip, axis=0, keepdims=False)
    total = keep + exchange(send.astype(jnp.bfloat16), 2).astype(jnp.float32)
    return total.astype(jnp.bfloat16)


def solution(mesh):
    placed = (
        P("seq", "chan"),
        P("seq", "chan"),
        P("seq", "chan"),
        P("seq", "chan"),
        P(),
        P(),
        P(),
        P(),
        P(),
        P("chan", None),
    )
    return jax.shard_map(
        per_device, mesh=mesh, in_specs=placed, out_specs=P(("seq", "chan"), None), check_vma=False
    )
```

```python
import jax
import jax.numpy as jnp
from jax import lax
from jax.sharding import PartitionSpec as P

ROW_SPLIT = 8


def to_columns(values, count):
    n, nb, blk, chans = values.shape
    cs = count // ROW_SPLIT
    parts = values.reshape(n, nb, ROW_SPLIT, blk // ROW_SPLIT, cs, chans // cs)
    parts = parts.transpose(2, 4, 0, 1, 3, 5).reshape(count, n, nb, blk // ROW_SPLIT, chans // cs)
    return lax.all_to_all(parts, "seq", 0, 0, tiled=True)


def from_columns(values, count, blk, chans):
    nb = values.shape[1]
    cs = count // ROW_SPLIT
    back = lax.all_to_all(values, "seq", 0, 0, tiled=True)
    back = back.reshape(ROW_SPLIT, cs, nb, blk // ROW_SPLIT, chans // cs)
    return back.transpose(2, 0, 3, 1, 4).reshape(nb, blk, chans)


def rotate_bit(values, cosine, sine, bit, sections, sign):
    axis = sections - 1 - bit
    lower = lax.index_in_dim(values, 0, axis, keepdims=True)
    upper = lax.index_in_dim(values, 1, axis, keepdims=True)
    new_lower = cosine * lower + sign * sine * upper
    new_upper = cosine * upper - sign * sine * lower
    return jnp.concatenate([new_lower, new_upper], axis=axis)


def per_device(
    value_in,
    gate_in,
    gate_out,
    spectral_filter,
    analysis_blocks,
    analysis_mix,
    synthesis_blocks,
    synthesis_mix,
    angles,
    out_weight,
):
    tokens, chans = value_in.shape
    nblocks = analysis_blocks.shape[0]
    blk = analysis_blocks.shape[1]
    count = lax.axis_size("seq")
    sections = count.bit_length() - 1
    rank = lax.axis_index("seq")
    mixed = (
        (gate_in.astype(jnp.float32) * value_in.astype(jnp.float32))
        .astype(jnp.bfloat16)
        .reshape(nblocks, blk, chans)
    )
    inner = jnp.einsum(
        "kij,kjc->kic", analysis_blocks, mixed, preferred_element_type=jnp.float32
    ).astype(jnp.bfloat16)
    spec = jnp.einsum(
        "ikl,lic->kic", analysis_mix, inner, preferred_element_type=jnp.float32
    ).astype(jnp.bfloat16)

    both = jnp.stack([spec, spectral_filter.reshape(nblocks, blk, chans)])
    both_cols = to_columns(both, count)
    spec_cols = both_cols[:, 0]
    filt_cols = both_cols[:, 1]
    rows = blk // ROW_SPLIT
    row_part = rank // (count // ROW_SPLIT)
    theta = angles.reshape(sections, nblocks, ROW_SPLIT, rows)
    theta = lax.dynamic_index_in_dim(theta, row_part, axis=2, keepdims=False)
    cosines = jnp.cos(theta)[:, :, :, None]
    sines = jnp.sin(theta)[:, :, :, None]

    shape = (2,) * sections + spec_cols.shape[1:]
    work = spec_cols.astype(jnp.float32).reshape(shape)
    for section in range(sections):
        work = rotate_bit(work, cosines[section], sines[section], section, sections, 1.0)
    work = work * filt_cols.astype(jnp.float32).reshape(shape)
    for section in reversed(range(sections)):
        work = rotate_bit(work, cosines[section], sines[section], section, sections, -1.0)
    work = work.astype(jnp.bfloat16).reshape(spec_cols.shape)

    grid = from_columns(work, count, blk, chans)
    spread = jnp.einsum(
        "ikl,lic->kic", synthesis_mix, grid, preferred_element_type=jnp.float32
    ).astype(jnp.bfloat16)
    conv = jnp.einsum("kij,kjc->kic", synthesis_blocks, spread, preferred_element_type=jnp.float32)
    gated = (gate_out.astype(jnp.float32) * conv.reshape(tokens, chans)).astype(jnp.bfloat16)
    product = jnp.dot(gated, out_weight, preferred_element_type=jnp.float32).astype(jnp.bfloat16)
    return scatter_sum(product)


def exchange(value, distance):
    pairs = [(source, source ^ distance) for source in range(lax.axis_size("chan"))]
    return lax.ppermute(value, "chan", pairs)


def scatter_sum(product):
    me = lax.axis_index("chan")
    core = me % 2
    chip = me // 2
    rows, width = product.shape
    quarters = product.reshape(2, 2, rows // 4, width)
    keep = lax.dynamic_index_in_dim(quarters, core, axis=1, keepdims=False)
    send = lax.dynamic_index_in_dim(quarters, 1 - core, axis=1, keepdims=False)
    half = keep.astype(jnp.float32) + exchange(send, 1).astype(jnp.float32)
    keep = lax.dynamic_index_in_dim(half, chip, axis=0, keepdims=False)
    send = lax.dynamic_index_in_dim(half, 1 - chip, axis=0, keepdims=False)
    total = keep + exchange(send.astype(jnp.bfloat16), 2).astype(jnp.float32)
    return total.astype(jnp.bfloat16)


def solution(mesh):
    placed = (
        P("seq", "chan"),
        P("seq", "chan"),
        P("seq", "chan"),
        P("seq", "chan"),
        P(),
        P(),
        P(),
        P(),
        P(),
        P("chan", None),
    )
    return jax.shard_map(
        per_device, mesh=mesh, in_specs=placed, out_specs=P(("seq", "chan"), None), check_vma=False
    )
```

```python
import jax
import jax.numpy as jnp
from jax import lax
from jax.sharding import PartitionSpec as P

ROW_SPLIT = 8


def to_columns(values, count):
    n, nb, blk, chans = values.shape
    cs = count // ROW_SPLIT
    parts = values.reshape(n, nb, ROW_SPLIT, blk // ROW_SPLIT, cs, chans // cs)
    parts = parts.transpose(2, 4, 0, 1, 3, 5).reshape(count, n, nb, blk // ROW_SPLIT, chans // cs)
    return lax.all_to_all(parts, "seq", 0, 0, tiled=True)


def from_columns(values, count, blk, chans):
    nb = values.shape[1]
    cs = count // ROW_SPLIT
    back = lax.all_to_all(values, "seq", 0, 0, tiled=True)
    back = back.reshape(ROW_SPLIT, cs, nb, blk // ROW_SPLIT, chans // cs)
    return back.transpose(2, 0, 3, 1, 4).reshape(nb, blk, chans)


def rotate_bit(values, cosine, sine, bit, sections, sign):
    axis = sections - 1 - bit
    lower = lax.index_in_dim(values, 0, axis, keepdims=True)
    upper = lax.index_in_dim(values, 1, axis, keepdims=True)
    new_lower = cosine * lower + sign * sine * upper
    new_upper = cosine * upper - sign * sine * lower
    return jnp.concatenate([new_lower, new_upper], axis=axis)


def per_device(
    value_in,
    gate_in,
    gate_out,
    spectral_filter,
    analysis_blocks,
    analysis_mix,
    synthesis_blocks,
    synthesis_mix,
    angles,
    out_weight,
):
    tokens, chans = value_in.shape
    nblocks = analysis_blocks.shape[0]
    blk = analysis_blocks.shape[1]
    count = lax.axis_size("seq")
    sections = count.bit_length() - 1
    rank = lax.axis_index("seq")
    mixed = (
        (gate_in.astype(jnp.float32) * value_in.astype(jnp.float32))
        .astype(jnp.bfloat16)
        .reshape(nblocks, blk, chans)
    )
    inner = jnp.einsum(
        "kij,kjc->kic", analysis_blocks, mixed, preferred_element_type=jnp.float32
    ).astype(jnp.bfloat16)
    spec = jnp.einsum(
        "ikl,lic->kic", analysis_mix, inner, preferred_element_type=jnp.float32
    ).astype(jnp.bfloat16)

    both = jnp.stack([spec, spectral_filter.reshape(nblocks, blk, chans)])
    both_cols = to_columns(both, count)
    spec_cols = both_cols[:, 0]
    filt_cols = both_cols[:, 1]
    rows = blk // ROW_SPLIT
    row_part = rank // (count // ROW_SPLIT)
    theta = angles.reshape(sections, nblocks, ROW_SPLIT, rows)
    theta = lax.dynamic_index_in_dim(theta, row_part, axis=2, keepdims=False)
    cosines = jnp.cos(theta)[:, :, :, None]
    sines = jnp.sin(theta)[:, :, :, None]

    shape = (2,) * sections + spec_cols.shape[1:]
    work = spec_cols.astype(jnp.float32).reshape(shape)
    for section in range(sections):
        work = rotate_bit(work, cosines[section], sines[section], section, sections, 1.0)
    work = work * filt_cols.astype(jnp.float32).reshape(shape)
    for section in reversed(range(sections)):
        work = rotate_bit(work, cosines[section], sines[section], section, sections, -1.0)
    work = work.astype(jnp.bfloat16).reshape(spec_cols.shape)

    grid = from_columns(work, count, blk, chans)
    spread = jnp.einsum(
        "ikl,lic->kic", synthesis_mix, grid, preferred_element_type=jnp.float32
    ).astype(jnp.bfloat16)
    conv = jnp.einsum("kij,kjc->kic", synthesis_blocks, spread, preferred_element_type=jnp.float32)
    gated = (gate_out.astype(jnp.float32) * conv.reshape(tokens, chans)).astype(jnp.bfloat16)
    return scatter_sum(gated, out_weight)


def exchange(value, distance):
    pairs = [(source, source ^ distance) for source in range(lax.axis_size("chan"))]
    return lax.ppermute(value, "chan", pairs)


def scatter_sum(gated, out_weight):
    me = lax.axis_index("chan")
    core = me % 2
    chip = me // 2
    rows, chans = gated.shape
    quarters = gated.reshape(2, 2, rows // 4, chans)
    sent_rows = lax.dynamic_index_in_dim(quarters, 1 - core, axis=1, keepdims=False)
    kept_rows = lax.dynamic_index_in_dim(quarters, core, axis=1, keepdims=False)
    sent = jnp.einsum("yrc,cw->yrw", sent_rows, out_weight, preferred_element_type=jnp.float32)
    half = exchange(sent.astype(jnp.bfloat16), 1)
    kept = jnp.einsum("yrc,cw->yrw", kept_rows, out_weight, preferred_element_type=jnp.float32)
    other = lax.dynamic_index_in_dim(kept, 1 - chip, axis=0, keepdims=False)
    other = other + lax.dynamic_index_in_dim(half, 1 - chip, axis=0, keepdims=False).astype(jnp.float32)
    quarter = exchange(other.astype(jnp.bfloat16), 2)
    mine = lax.dynamic_index_in_dim(kept, chip, axis=0, keepdims=False)
    mine = mine + lax.dynamic_index_in_dim(half, chip, axis=0, keepdims=False).astype(jnp.float32)
    return (mine + quarter.astype(jnp.float32)).astype(jnp.bfloat16)


def solution(mesh):
    placed = (
        P("seq", "chan"),
        P("seq", "chan"),
        P("seq", "chan"),
        P("seq", "chan"),
        P(),
        P(),
        P(),
        P(),
        P(),
        P("chan", None),
    )
    return jax.shard_map(
        per_device, mesh=mesh, in_specs=placed, out_specs=P(("seq", "chan"), None), check_vma=False
    )
```

```python
import jax
import jax.numpy as jnp
from jax import lax
from jax.sharding import PartitionSpec as P

ROW_SPLIT = 8


def to_columns(values, count):
    n, nb, blk, chans = values.shape
    cs = count // ROW_SPLIT
    parts = values.reshape(n, nb, ROW_SPLIT, blk // ROW_SPLIT, cs, chans // cs)
    parts = parts.transpose(2, 4, 0, 1, 3, 5).reshape(count, n, nb, blk // ROW_SPLIT, chans // cs)
    return lax.all_to_all(parts, "seq", 0, 0, tiled=True)


def from_columns(values, count, blk, chans):
    nb = values.shape[1]
    cs = count // ROW_SPLIT
    back = lax.all_to_all(values, "seq", 0, 0, tiled=True)
    back = back.reshape(ROW_SPLIT, cs, nb, blk // ROW_SPLIT, chans // cs)
    return back.transpose(2, 0, 3, 1, 4).reshape(nb, blk, chans)


def per_device(
    value_in,
    gate_in,
    gate_out,
    spectral_filter,
    analysis_blocks,
    analysis_mix,
    synthesis_blocks,
    synthesis_mix,
    angles,
    out_weight,
):
    tokens, chans = value_in.shape
    nblocks = analysis_blocks.shape[0]
    blk = analysis_blocks.shape[1]
    count = lax.axis_size("seq")
    sections = count.bit_length() - 1
    rank = lax.axis_index("seq")
    mixed = (
        (gate_in.astype(jnp.float32) * value_in.astype(jnp.float32))
        .astype(jnp.bfloat16)
        .reshape(nblocks, blk, chans)
    )
    inner = jnp.einsum(
        "kij,kjc->kic", analysis_blocks, mixed, preferred_element_type=jnp.float32
    ).astype(jnp.bfloat16)
    spec = jnp.einsum(
        "ikl,lic->kic", analysis_mix, inner, preferred_element_type=jnp.float32
    ).astype(jnp.bfloat16)

    both = jnp.stack([spec, spectral_filter.reshape(nblocks, blk, chans)])
    both_cols = to_columns(both, count)
    spec_cols = both_cols[:, 0]
    filt_cols = both_cols[:, 1]
    rows = blk // ROW_SPLIT
    row_part = rank // (count // ROW_SPLIT)
    theta = angles.reshape(sections, nblocks, ROW_SPLIT, rows)
    theta = lax.dynamic_index_in_dim(theta, row_part, axis=2, keepdims=False)
    cosines = jnp.cos(theta)[:, :, :, None]
    sines = jnp.sin(theta)[:, :, :, None]

    bits = (jnp.arange(count)[:, None] >> jnp.arange(sections)[None, :]) & 1
    same = bits[:, None, :] == bits[None, :, :]
    below = (bits[:, None, :] == 0) & (bits[None, :, :] == 1)
    factor = jnp.where(
        same[None, None],
        cosines[..., 0].transpose(1, 2, 0)[:, :, None, None, :],
        jnp.where(below[None, None], 1.0, -1.0) * sines[..., 0].transpose(1, 2, 0)[:, :, None, None, :],
    )
    matrix = jnp.prod(factor, axis=-1)
    hi = lax.Precision.HIGHEST
    work = jnp.einsum("kide,ekic->dkic", matrix, spec_cols.astype(jnp.float32), precision=hi)
    work = work * filt_cols.astype(jnp.float32)
    work = jnp.einsum("kied,ekic->dkic", matrix, work, precision=hi)
    work = work.astype(jnp.bfloat16)

    grid = from_columns(work, count, blk, chans)
    spread = jnp.einsum(
        "ikl,lic->kic", synthesis_mix, grid, preferred_element_type=jnp.float32
    ).astype(jnp.bfloat16)
    conv = jnp.einsum("kij,kjc->kic", synthesis_blocks, spread, preferred_element_type=jnp.float32)
    gated = (gate_out.astype(jnp.float32) * conv.reshape(tokens, chans)).astype(jnp.bfloat16)
    return scatter_sum(gated, out_weight)


def exchange(value, distance):
    pairs = [(source, source ^ distance) for source in range(lax.axis_size("chan"))]
    return lax.ppermute(value, "chan", pairs)


def scatter_sum(gated, out_weight):
    me = lax.axis_index("chan")
    core = me % 2
    chip = me // 2
    rows, chans = gated.shape
    quarters = gated.reshape(2, 2, rows // 4, chans)
    sent_rows = lax.dynamic_index_in_dim(quarters, 1 - core, axis=1, keepdims=False)
    kept_rows = lax.dynamic_index_in_dim(quarters, core, axis=1, keepdims=False)
    sent = jnp.einsum("yrc,cw->yrw", sent_rows, out_weight, preferred_element_type=jnp.float32)
    half = exchange(sent.astype(jnp.bfloat16), 1)
    kept = jnp.einsum("yrc,cw->yrw", kept_rows, out_weight, preferred_element_type=jnp.float32)
    other = lax.dynamic_index_in_dim(kept, 1 - chip, axis=0, keepdims=False)
    other = other + lax.dynamic_index_in_dim(half, 1 - chip, axis=0, keepdims=False).astype(jnp.float32)
    quarter = exchange(other.astype(jnp.bfloat16), 2)
    mine = lax.dynamic_index_in_dim(kept, chip, axis=0, keepdims=False)
    mine = mine + lax.dynamic_index_in_dim(half, chip, axis=0, keepdims=False).astype(jnp.float32)
    return (mine + quarter.astype(jnp.float32)).astype(jnp.bfloat16)


def solution(mesh):
    placed = (
        P("seq", "chan"),
        P("seq", "chan"),
        P("seq", "chan"),
        P("seq", "chan"),
        P(),
        P(),
        P(),
        P(),
        P(),
        P("chan", None),
    )
    return jax.shard_map(
        per_device, mesh=mesh, in_specs=placed, out_specs=P(("seq", "chan"), None), check_vma=False
    )
```

```python
import jax
import jax.numpy as jnp
from jax import lax
from jax.sharding import PartitionSpec as P

ROW_SPLIT = 8


def to_columns(values, count):
    n, nb, blk, chans = values.shape
    cs = count // ROW_SPLIT
    parts = values.reshape(n, nb, ROW_SPLIT, blk // ROW_SPLIT, cs, chans // cs)
    parts = parts.transpose(2, 4, 0, 1, 3, 5).reshape(count, n, nb, blk // ROW_SPLIT, chans // cs)
    return lax.all_to_all(parts, "seq", 0, 0, tiled=True)


def from_columns(values, count, blk, chans):
    nb = values.shape[1]
    cs = count // ROW_SPLIT
    back = lax.all_to_all(values, "seq", 0, 0, tiled=True)
    back = back.reshape(ROW_SPLIT, cs, nb, blk // ROW_SPLIT, chans // cs)
    return back.transpose(2, 0, 3, 1, 4).reshape(nb, blk, chans)


def per_device(
    value_in,
    gate_in,
    gate_out,
    spectral_filter,
    analysis_blocks,
    analysis_mix,
    synthesis_blocks,
    synthesis_mix,
    angles,
    out_weight,
):
    tokens, chans = value_in.shape
    nblocks = analysis_blocks.shape[0]
    blk = analysis_blocks.shape[1]
    count = lax.axis_size("seq")
    sections = count.bit_length() - 1
    rank = lax.axis_index("seq")
    mixed = (
        (gate_in.astype(jnp.float32) * value_in.astype(jnp.float32))
        .astype(jnp.bfloat16)
        .reshape(nblocks, blk, chans)
    )
    inner = jnp.einsum(
        "kij,kjc->kic", analysis_blocks, mixed, preferred_element_type=jnp.float32
    ).astype(jnp.bfloat16)
    spec = jnp.einsum(
        "ikl,lic->kic", analysis_mix, inner, preferred_element_type=jnp.float32
    ).astype(jnp.bfloat16)

    both = jnp.stack([spec, spectral_filter.reshape(nblocks, blk, chans)])
    both_cols = to_columns(both, count)
    spec_cols = both_cols[:, 0]
    filt_cols = both_cols[:, 1]
    rows = blk // ROW_SPLIT
    row_part = rank // (count // ROW_SPLIT)
    theta = angles.reshape(sections, nblocks, ROW_SPLIT, rows)
    theta = lax.dynamic_index_in_dim(theta, row_part, axis=2, keepdims=False)
    cosines = jnp.cos(theta)[:, :, :, None]
    sines = jnp.sin(theta)[:, :, :, None]

    bits = (jnp.arange(count)[:, None] >> jnp.arange(sections)[None, :]) & 1
    same = bits[:, None, :] == bits[None, :, :]
    below = (bits[:, None, :] == 0) & (bits[None, :, :] == 1)
    factor = jnp.where(
        same[None, None],
        cosines[..., 0].transpose(1, 2, 0)[:, :, None, None, :],
        jnp.where(below[None, None], 1.0, -1.0) * sines[..., 0].transpose(1, 2, 0)[:, :, None, None, :],
    )
    matrix = jnp.prod(factor, axis=-1)
    hi = lax.Precision.HIGHEST
    work = jnp.einsum("kide,ekic->dkic", matrix, spec_cols.astype(jnp.float32), precision=hi)
    work = work * filt_cols.astype(jnp.float32)
    work = jnp.einsum("kied,ekic->dkic", matrix, work, precision=hi)
    work = work.astype(jnp.bfloat16)

    grid = from_columns(work, count, blk, chans)
    spread = jnp.einsum(
        "ikl,lic->kic", synthesis_mix, grid, preferred_element_type=jnp.float32
    ).astype(jnp.bfloat16)
    conv = jnp.einsum("kij,kjc->kic", synthesis_blocks, spread, preferred_element_type=jnp.float32)
    gated = (gate_out.astype(jnp.float32) * conv.reshape(tokens, chans)).astype(jnp.bfloat16)
    return scatter_sum(gated, out_weight)


def exchange(value, distance):
    pairs = [(source, source ^ distance) for source in range(lax.axis_size("chan"))]
    return lax.ppermute(value, "chan", pairs)


def scatter_sum(gated, out_weight, blocks=4):
    me = lax.axis_index("chan")
    core = me % 2
    chip = me // 2
    rows, chans = gated.shape
    width = out_weight.shape[1] // blocks
    pieces = []
    for block in range(blocks):
        weight = out_weight[:, block * width : (block + 1) * width]
        product = jnp.dot(gated, weight, preferred_element_type=jnp.float32)
        quarters = product.reshape(2, 2, rows // 4, width)
        sent = lax.dynamic_index_in_dim(quarters, 1 - core, axis=1, keepdims=False)
        kept = lax.dynamic_index_in_dim(quarters, core, axis=1, keepdims=False)
        half = exchange(sent.astype(jnp.bfloat16), 1)
        gated, half = lax.optimization_barrier((gated, half))
        other = lax.dynamic_index_in_dim(kept, 1 - chip, axis=0, keepdims=False)
        other = other + lax.dynamic_index_in_dim(half, 1 - chip, axis=0, keepdims=False).astype(jnp.float32)
        quarter = exchange(other.astype(jnp.bfloat16), 2)
        mine = lax.dynamic_index_in_dim(kept, chip, axis=0, keepdims=False)
        mine = mine + lax.dynamic_index_in_dim(half, chip, axis=0, keepdims=False).astype(jnp.float32)
        pieces.append((mine + quarter.astype(jnp.float32)).astype(jnp.bfloat16))
    return jnp.concatenate(pieces, axis=1)


def solution(mesh):
    placed = (
        P("seq", "chan"),
        P("seq", "chan"),
        P("seq", "chan"),
        P("seq", "chan"),
        P(),
        P(),
        P(),
        P(),
        P(),
        P("chan", None),
    )
    return jax.shard_map(
        per_device, mesh=mesh, in_specs=placed, out_specs=P(("seq", "chan"), None), check_vma=False
    )
```

```python
import jax
import jax.numpy as jnp
from jax import lax
from jax.sharding import PartitionSpec as P


ROW_SPLIT = 8


def to_columns(values, count):
    n, nb, blk, chans = values.shape
    cs = count // ROW_SPLIT
    parts = values.reshape(n, nb, ROW_SPLIT, blk // ROW_SPLIT, cs, chans // cs)
    parts = parts.transpose(2, 4, 0, 1, 3, 5).reshape(count, n, nb, blk // ROW_SPLIT, chans // cs)
    return lax.all_to_all(parts, "seq", 0, 0, tiled=True)


def from_columns(values, count, blk, chans):
    nb = values.shape[1]
    cs = count // ROW_SPLIT
    back = lax.all_to_all(values, "seq", 0, 0, tiled=True)
    back = back.reshape(ROW_SPLIT, cs, nb, blk // ROW_SPLIT, chans // cs)
    return back.transpose(2, 0, 3, 1, 4).reshape(nb, blk, chans)


def per_device(
    value_in,
    gate_in,
    gate_out,
    spectral_filter,
    analysis_blocks,
    analysis_mix,
    synthesis_blocks,
    synthesis_mix,
    angles,
    out_weight,
):
    tokens, chans = value_in.shape
    nblocks = analysis_blocks.shape[0]
    blk = analysis_blocks.shape[1]
    count = lax.axis_size("seq")
    sections = count.bit_length() - 1
    rank = lax.axis_index("seq")
    mixed = (
        (gate_in.astype(jnp.float32) * value_in.astype(jnp.float32))
        .astype(jnp.bfloat16)
        .reshape(nblocks, blk, chans)
    )
    inner = jnp.einsum(
        "kij,kjc->kic", analysis_blocks, mixed, preferred_element_type=jnp.float32
    ).astype(jnp.bfloat16)
    spec = jnp.einsum(
        "ikl,lic->kic", analysis_mix, inner, preferred_element_type=jnp.float32
    ).astype(jnp.bfloat16)

    both = jnp.stack([spec, spectral_filter.reshape(nblocks, blk, chans)])
    both_cols = to_columns(both, count)
    spec_cols = both_cols[:, 0]
    filt_cols = both_cols[:, 1]
    rows = blk // ROW_SPLIT
    row_part = rank // (count // ROW_SPLIT)
    theta = angles.reshape(sections, nblocks, ROW_SPLIT, rows)
    theta = lax.dynamic_index_in_dim(theta, row_part, axis=2, keepdims=False)
    cosines = jnp.cos(theta)[:, :, :, None]
    sines = jnp.sin(theta)[:, :, :, None]

    bits = (jnp.arange(count)[:, None] >> jnp.arange(sections)[None, :]) & 1
    same = bits[:, None, :] == bits[None, :, :]
    below = (bits[:, None, :] == 0) & (bits[None, :, :] == 1)
    factor = jnp.where(
        same[None, None],
        cosines[..., 0].transpose(1, 2, 0)[:, :, None, None, :],
        jnp.where(below[None, None], 1.0, -1.0) * sines[..., 0].transpose(1, 2, 0)[:, :, None, None, :],
    )
    matrix = jnp.prod(factor, axis=-1)
    hi = lax.Precision.HIGHEST
    work = jnp.einsum("kide,ekic->dkic", matrix, spec_cols.astype(jnp.float32), precision=hi)
    work = work * filt_cols.astype(jnp.float32)
    work = jnp.einsum("kied,ekic->dkic", matrix, work, precision=hi)
    work = work.astype(jnp.bfloat16)

    grid = from_columns(work, count, blk, chans)
    spread = jnp.einsum(
        "ikl,lic->kic", synthesis_mix, grid, preferred_element_type=jnp.float32
    ).astype(jnp.bfloat16)
    conv = jnp.einsum("kij,kjc->kic", synthesis_blocks, spread, preferred_element_type=jnp.float32)
    gated = (gate_out.astype(jnp.float32) * conv.reshape(tokens, chans)).astype(jnp.bfloat16)
    return scatter_sum(gated, out_weight)


def exchange(value, distance):
    pairs = [(source, source ^ distance) for source in range(lax.axis_size("chan"))]
    return lax.ppermute(value, "chan", pairs)


def scatter_sum(gated, out_weight, blocks=4):
    me = lax.axis_index("chan")
    core = me % 2
    chip = me // 2
    width = out_weight.shape[1] // blocks
    pieces = []
    for block in range(blocks):
        pieces.append(scatter_block(gated, out_weight, block, width, core, chip))
        gated = pieces[-1][1]
    return jnp.concatenate([piece for piece, _ in pieces], axis=1)


def scatter_block(gated, out_weight, block, width, core, chip):
    rows = gated.shape[0]
    weight = out_weight[:, block * width : (block + 1) * width]
    product = jnp.dot(gated, weight, preferred_element_type=jnp.float32)
    quarters = product.reshape(2, 2, rows // 4, width)
    sent = lax.dynamic_index_in_dim(quarters, 1 - core, axis=1, keepdims=False)
    kept = lax.dynamic_index_in_dim(quarters, core, axis=1, keepdims=False)
    half = exchange(sent.astype(jnp.bfloat16), 1)
    other = lax.dynamic_index_in_dim(kept, 1 - chip, axis=0, keepdims=False)
    other = other + lax.dynamic_index_in_dim(half, 1 - chip, axis=0, keepdims=False).astype(jnp.float32)
    gated, other = lax.optimization_barrier((gated, other.astype(jnp.bfloat16)))
    quarter = exchange(other, 2)
    mine = lax.dynamic_index_in_dim(kept, chip, axis=0, keepdims=False)
    mine = mine + lax.dynamic_index_in_dim(half, chip, axis=0, keepdims=False).astype(jnp.float32)
    return (mine + quarter.astype(jnp.float32)).astype(jnp.bfloat16), gated


def solution(mesh):
    placed = (
        P("seq", "chan"),
        P("seq", "chan"),
        P("seq", "chan"),
        P("seq", "chan"),
        P(),
        P(),
        P(),
        P(),
        P(),
        P("chan", None),
    )
    return jax.shard_map(
        per_device, mesh=mesh, in_specs=placed, out_specs=P(("seq", "chan"), None), check_vma=False
    )
```

```python
import jax
import jax.numpy as jnp
from jax import lax
from jax.sharding import PartitionSpec as P


ROW_SPLIT = 8


def to_columns(values, count):
    n, nb, blk, chans = values.shape
    cs = count // ROW_SPLIT
    parts = values.reshape(n, nb, ROW_SPLIT, blk // ROW_SPLIT, cs, chans // cs)
    parts = parts.transpose(2, 4, 0, 1, 3, 5).reshape(count, n, nb, blk // ROW_SPLIT, chans // cs)
    return lax.all_to_all(parts, "seq", 0, 0, tiled=True)


def from_columns(values, count, blk, chans):
    nb = values.shape[1]
    cs = count // ROW_SPLIT
    back = lax.all_to_all(values, "seq", 0, 0, tiled=True)
    back = back.reshape(ROW_SPLIT, cs, nb, blk // ROW_SPLIT, chans // cs)
    return back.transpose(2, 0, 3, 1, 4).reshape(nb, blk, chans)


def per_device(
    value_in,
    gate_in,
    gate_out,
    spectral_filter,
    analysis_blocks,
    analysis_mix,
    synthesis_blocks,
    synthesis_mix,
    angles,
    out_weight,
):
    tokens, chans = value_in.shape
    nblocks = analysis_blocks.shape[0]
    blk = analysis_blocks.shape[1]
    count = lax.axis_size("seq")
    sections = count.bit_length() - 1
    rank = lax.axis_index("seq")
    mixed = (
        (gate_in.astype(jnp.float32) * value_in.astype(jnp.float32))
        .astype(jnp.bfloat16)
        .reshape(nblocks, blk, chans)
    )
    inner = jnp.einsum(
        "kij,kjc->kic", analysis_blocks, mixed, preferred_element_type=jnp.float32
    ).astype(jnp.bfloat16)
    spec = jnp.einsum(
        "ikl,lic->kic", analysis_mix, inner, preferred_element_type=jnp.float32
    ).astype(jnp.bfloat16)

    both = jnp.stack([spec, spectral_filter.reshape(nblocks, blk, chans)])
    both_cols = to_columns(both, count)
    spec_cols = both_cols[:, 0]
    filt_cols = both_cols[:, 1]
    rows = blk // ROW_SPLIT
    row_part = rank // (count // ROW_SPLIT)
    theta = angles.reshape(sections, nblocks, ROW_SPLIT, rows)
    theta = lax.dynamic_index_in_dim(theta, row_part, axis=2, keepdims=False)
    cosines = jnp.cos(theta)[:, :, :, None]
    sines = jnp.sin(theta)[:, :, :, None]

    bits = (jnp.arange(count)[:, None] >> jnp.arange(sections)[None, :]) & 1
    same = bits[:, None, :] == bits[None, :, :]
    below = (bits[:, None, :] == 0) & (bits[None, :, :] == 1)
    factor = jnp.where(
        same[None, None],
        cosines[..., 0].transpose(1, 2, 0)[:, :, None, None, :],
        jnp.where(below[None, None], 1.0, -1.0) * sines[..., 0].transpose(1, 2, 0)[:, :, None, None, :],
    )
    matrix = jnp.prod(factor, axis=-1)
    hi = lax.Precision.HIGHEST
    work = jnp.einsum("kide,ekic->dkic", matrix, spec_cols.astype(jnp.float32), precision=hi)
    work = work * filt_cols.astype(jnp.float32)
    work = jnp.einsum("kied,ekic->dkic", matrix, work, precision=hi)
    work = work.astype(jnp.bfloat16)

    grid = from_columns(work, count, blk, chans)
    spread = jnp.einsum(
        "ikl,lic->kic", synthesis_mix, grid, preferred_element_type=jnp.float32
    ).astype(jnp.bfloat16)
    conv = jnp.einsum("kij,kjc->kic", synthesis_blocks, spread, preferred_element_type=jnp.float32)
    gated = (gate_out.astype(jnp.float32) * conv.reshape(tokens, chans)).astype(jnp.bfloat16)
    return scatter_sum(gated, out_weight)


def exchange(value, distance):
    pairs = [(source, source ^ distance) for source in range(lax.axis_size("chan"))]
    return lax.ppermute(value, "chan", pairs)


BLOCKS = 8


def scatter_sum(gated, out_weight, blocks=BLOCKS):
    me = lax.axis_index("chan")
    core = me % 2
    chip = me // 2
    width = out_weight.shape[1] // blocks
    pieces = []
    for block in range(blocks):
        pieces.append(scatter_block(gated, out_weight, block, width, core, chip))
    return jnp.concatenate(pieces, axis=1)


def scatter_block(gated, out_weight, block, width, core, chip):
    rows = gated.shape[0]
    weight = out_weight[:, block * width : (block + 1) * width]
    product = jnp.dot(gated, weight, preferred_element_type=jnp.float32)
    quarters = product.reshape(2, 2, rows // 4, width)
    sent = lax.dynamic_index_in_dim(quarters, 1 - core, axis=1, keepdims=False)
    kept = lax.dynamic_index_in_dim(quarters, core, axis=1, keepdims=False)
    half = exchange(sent.astype(jnp.bfloat16), 1)
    other = lax.dynamic_index_in_dim(kept, 1 - chip, axis=0, keepdims=False)
    other = other + lax.dynamic_index_in_dim(half, 1 - chip, axis=0, keepdims=False).astype(jnp.float32)
    quarter = exchange(other.astype(jnp.bfloat16), 2)
    mine = lax.dynamic_index_in_dim(kept, chip, axis=0, keepdims=False)
    mine = mine + lax.dynamic_index_in_dim(half, chip, axis=0, keepdims=False).astype(jnp.float32)
    return (mine + quarter.astype(jnp.float32)).astype(jnp.bfloat16)


def solution(mesh):
    placed = (
        P("seq", "chan"),
        P("seq", "chan"),
        P("seq", "chan"),
        P("seq", "chan"),
        P(),
        P(),
        P(),
        P(),
        P(),
        P("chan", None),
    )
    return jax.shard_map(
        per_device, mesh=mesh, in_specs=placed, out_specs=P(("seq", "chan"), None), check_vma=False
    )
```

```python
import jax
import jax.numpy as jnp
from jax import lax
from jax.experimental import pallas as pl
from jax.experimental.pallas import tpu as pltpu
from jax.sharding import PartitionSpec as P


ROW_SPLIT = 8


def prelude_kernel(gin_ref, vin_ref, filt_ref, blocks_ref, mix_ref, out_ref):
    nb, blk = blocks_ref.shape[0], blocks_ref.shape[1]
    count, rows, lanes = out_ref.shape[0], out_ref.shape[3], out_ref.shape[4]
    cs = count // (blk // rows)
    inner = []
    for k in range(nb):
        part = slice(k * blk, (k + 1) * blk)
        mixed = gin_ref[part, :].astype(jnp.float32) * vin_ref[part, :].astype(jnp.float32)
        inner.append(
            jnp.dot(blocks_ref[k], mixed.astype(jnp.bfloat16), preferred_element_type=jnp.float32)
            .astype(jnp.bfloat16)
            .astype(jnp.float32)
        )
    for k in range(nb):
        acc = mix_ref[:, k * nb : k * nb + 1] * inner[0]
        for l in range(1, nb):
            acc = acc + mix_ref[:, k * nb + l : k * nb + l + 1] * inner[l]
        spec = acc.astype(jnp.bfloat16)
        for a in range(blk // rows):
            for b in range(cs):
                cols = slice(b * lanes, (b + 1) * lanes)
                out_ref[a * cs + b, 0, k] = spec[a * rows : (a + 1) * rows, cols]
                out_ref[a * cs + b, 1, k] = filt_ref[k * blk + a * rows : k * blk + (a + 1) * rows, cols]


def prelude(gate_in, value_in, spectral_filter, blocks, mix, count):
    tokens, chans = gate_in.shape
    nb, blk = blocks.shape[0], blocks.shape[1]
    cs = count // ROW_SPLIT
    vmem = pl.BlockSpec(memory_space=pltpu.VMEM)
    return pl.pallas_call(
        prelude_kernel,
        out_shape=jax.ShapeDtypeStruct((count, 2, nb, blk // ROW_SPLIT, chans // cs), jnp.bfloat16),
        in_specs=[vmem] * 5,
        out_specs=vmem,
        cost_estimate=pl.CostEstimate(
            flops=2 * tokens * blk * chans + 6 * nb * tokens * chans,
            bytes_accessed=2 * 5 * tokens * chans,
            transcendentals=0,
        ),
    )(gate_in, value_in, spectral_filter, blocks, mix.astype(jnp.float32).reshape(blk, nb * nb))


def from_columns(values, count, blk, chans):
    nb = values.shape[1]
    cs = count // ROW_SPLIT
    back = lax.all_to_all(values, "seq", 0, 0, tiled=True)
    back = back.reshape(ROW_SPLIT, cs, nb, blk // ROW_SPLIT, chans // cs)
    return back.transpose(2, 0, 3, 1, 4).reshape(nb, blk, chans)


def per_device(
    value_in,
    gate_in,
    gate_out,
    spectral_filter,
    analysis_blocks,
    analysis_mix,
    synthesis_blocks,
    synthesis_mix,
    angles,
    out_weight,
):
    tokens, chans = value_in.shape
    nblocks = analysis_blocks.shape[0]
    blk = analysis_blocks.shape[1]
    count = lax.axis_size("seq")
    sections = count.bit_length() - 1
    rank = lax.axis_index("seq")
    parts = prelude(gate_in, value_in, spectral_filter, analysis_blocks, analysis_mix, count)
    both_cols = lax.all_to_all(parts, "seq", 0, 0, tiled=True)
    spec_cols = both_cols[:, 0]
    filt_cols = both_cols[:, 1]
    rows = blk // ROW_SPLIT
    row_part = rank // (count // ROW_SPLIT)
    theta = angles.reshape(sections, nblocks, ROW_SPLIT, rows)
    theta = lax.dynamic_index_in_dim(theta, row_part, axis=2, keepdims=False)
    cosines = jnp.cos(theta)[:, :, :, None]
    sines = jnp.sin(theta)[:, :, :, None]

    bits = (jnp.arange(count)[:, None] >> jnp.arange(sections)[None, :]) & 1
    same = bits[:, None, :] == bits[None, :, :]
    below = (bits[:, None, :] == 0) & (bits[None, :, :] == 1)
    factor = jnp.where(
        same[None, None],
        cosines[..., 0].transpose(1, 2, 0)[:, :, None, None, :],
        jnp.where(below[None, None], 1.0, -1.0) * sines[..., 0].transpose(1, 2, 0)[:, :, None, None, :],
    )
    matrix = jnp.prod(factor, axis=-1)
    hi = lax.Precision.HIGHEST
    work = jnp.einsum("kide,ekic->dkic", matrix, spec_cols.astype(jnp.float32), precision=hi)
    work = work * filt_cols.astype(jnp.float32)
    work = jnp.einsum("kied,ekic->dkic", matrix, work, precision=hi)
    work = work.astype(jnp.bfloat16)

    grid = from_columns(work, count, blk, chans)
    spread = jnp.einsum(
        "ikl,lic->kic", synthesis_mix, grid, preferred_element_type=jnp.float32
    ).astype(jnp.bfloat16)
    conv = jnp.einsum("kij,kjc->kic", synthesis_blocks, spread, preferred_element_type=jnp.float32)
    gated = (gate_out.astype(jnp.float32) * conv.reshape(tokens, chans)).astype(jnp.bfloat16)
    return scatter_sum(gated, out_weight)


def exchange(value, distance):
    pairs = [(source, source ^ distance) for source in range(lax.axis_size("chan"))]
    return lax.ppermute(value, "chan", pairs)


def scatter_sum(gated, out_weight, blocks=4):
    me = lax.axis_index("chan")
    core = me % 2
    chip = me // 2
    width = out_weight.shape[1] // blocks
    pieces = []
    for block in range(blocks):
        pieces.append(scatter_block(gated, out_weight, block, width, core, chip))
    return jnp.concatenate(pieces, axis=1)


def scatter_block(gated, out_weight, block, width, core, chip):
    rows = gated.shape[0]
    weight = out_weight[:, block * width : (block + 1) * width]
    product = jnp.dot(gated, weight, preferred_element_type=jnp.float32)
    quarters = product.reshape(2, 2, rows // 4, width)
    sent = lax.dynamic_index_in_dim(quarters, 1 - core, axis=1, keepdims=False)
    kept = lax.dynamic_index_in_dim(quarters, core, axis=1, keepdims=False)
    half = exchange(sent.astype(jnp.bfloat16), 1)
    other = lax.dynamic_index_in_dim(kept, 1 - chip, axis=0, keepdims=False)
    other = other + lax.dynamic_index_in_dim(half, 1 - chip, axis=0, keepdims=False).astype(jnp.float32)
    quarter = exchange(other.astype(jnp.bfloat16), 2)
    mine = lax.dynamic_index_in_dim(kept, chip, axis=0, keepdims=False)
    mine = mine + lax.dynamic_index_in_dim(half, chip, axis=0, keepdims=False).astype(jnp.float32)
    return (mine + quarter.astype(jnp.float32)).astype(jnp.bfloat16)


def solution(mesh):
    placed = (
        P("seq", "chan"),
        P("seq", "chan"),
        P("seq", "chan"),
        P("seq", "chan"),
        P(),
        P(),
        P(),
        P(),
        P(),
        P("chan", None),
    )
    return jax.shard_map(
        per_device, mesh=mesh, in_specs=placed, out_specs=P(("seq", "chan"), None), check_vma=False
    )
```

```python
import jax
import jax.numpy as jnp
from jax import lax
from jax.experimental import pallas as pl
from jax.experimental.pallas import tpu as pltpu
from jax.sharding import PartitionSpec as P


ROW_SPLIT = 8


def prelude_kernel(gin_ref, vin_ref, filt_ref, blocks_ref, mix_ref, out_ref):
    nb, blk = blocks_ref.shape[0], blocks_ref.shape[1]
    count, rows, lanes = out_ref.shape[0], out_ref.shape[3], out_ref.shape[4]
    cs = count // (blk // rows)
    inner = []
    for k in range(nb):
        part = slice(k * blk, (k + 1) * blk)
        mixed = gin_ref[part, :].astype(jnp.float32) * vin_ref[part, :].astype(jnp.float32)
        inner.append(
            jnp.dot(blocks_ref[k], mixed.astype(jnp.bfloat16), preferred_element_type=jnp.float32)
            .astype(jnp.bfloat16)
            .astype(jnp.float32)
        )
    for k in range(nb):
        acc = mix_ref[:, k * nb : k * nb + 1] * inner[0]
        for l in range(1, nb):
            acc = acc + mix_ref[:, k * nb + l : k * nb + l + 1] * inner[l]
        spec = acc.astype(jnp.bfloat16)
        for a in range(blk // rows):
            for b in range(cs):
                cols = slice(b * lanes, (b + 1) * lanes)
                out_ref[a * cs + b, 0, k] = spec[a * rows : (a + 1) * rows, cols]
                out_ref[a * cs + b, 1, k] = filt_ref[k * blk + a * rows : k * blk + (a + 1) * rows, cols]


def prelude(gate_in, value_in, spectral_filter, blocks, mix, count):
    tokens, chans = gate_in.shape
    nb, blk = blocks.shape[0], blocks.shape[1]
    cs = count // ROW_SPLIT
    vmem = pl.BlockSpec(memory_space=pltpu.VMEM)
    return pl.pallas_call(
        prelude_kernel,
        out_shape=jax.ShapeDtypeStruct((count, 2, nb, blk // ROW_SPLIT, chans // cs), jnp.bfloat16),
        in_specs=[vmem] * 5,
        out_specs=vmem,
        cost_estimate=pl.CostEstimate(
            flops=2 * tokens * blk * chans + 6 * nb * tokens * chans,
            bytes_accessed=2 * 5 * tokens * chans,
            transcendentals=0,
        ),
    )(gate_in, value_in, spectral_filter, blocks, mix.astype(jnp.float32).reshape(blk, nb * nb))


def from_columns(values, count, blk, chans):
    nb = values.shape[1]
    cs = count // ROW_SPLIT
    back = lax.all_to_all(values, "seq", 0, 0, tiled=True)
    back = back.reshape(ROW_SPLIT, cs, nb, blk // ROW_SPLIT, chans // cs)
    return back.transpose(2, 0, 3, 1, 4).reshape(nb, blk, chans)


def rotate_bit(values, cosine, sine, bit, sections, sign):
    axis = sections - 1 - bit
    lower = lax.index_in_dim(values, 0, axis, keepdims=True)
    upper = lax.index_in_dim(values, 1, axis, keepdims=True)
    new_lower = cosine * lower + sign * sine * upper
    new_upper = cosine * upper - sign * sine * lower
    return jnp.concatenate([new_lower, new_upper], axis=axis)


def per_device(
    value_in,
    gate_in,
    gate_out,
    spectral_filter,
    analysis_blocks,
    analysis_mix,
    synthesis_blocks,
    synthesis_mix,
    angles,
    out_weight,
):
    tokens, chans = value_in.shape
    nblocks = analysis_blocks.shape[0]
    blk = analysis_blocks.shape[1]
    count = lax.axis_size("seq")
    sections = count.bit_length() - 1
    rank = lax.axis_index("seq")
    parts = prelude(gate_in, value_in, spectral_filter, analysis_blocks, analysis_mix, count)
    both_cols = lax.all_to_all(parts, "seq", 0, 0, tiled=True)
    spec_cols = both_cols[:, 0]
    filt_cols = both_cols[:, 1]
    rows = blk // ROW_SPLIT
    row_part = rank // (count // ROW_SPLIT)
    theta = angles.reshape(sections, nblocks, ROW_SPLIT, rows)
    theta = lax.dynamic_index_in_dim(theta, row_part, axis=2, keepdims=False)
    cosines = jnp.cos(theta)[:, :, :, None]
    sines = jnp.sin(theta)[:, :, :, None]

    shape = (2,) * sections + spec_cols.shape[1:]
    work = spec_cols.astype(jnp.float32).reshape(shape)
    for section in range(sections):
        work = rotate_bit(work, cosines[section], sines[section], section, sections, 1.0)
    work = work * filt_cols.astype(jnp.float32).reshape(shape)
    for section in reversed(range(sections)):
        work = rotate_bit(work, cosines[section], sines[section], section, sections, -1.0)
    work = work.astype(jnp.bfloat16).reshape(spec_cols.shape)

    grid = from_columns(work, count, blk, chans)
    spread = jnp.einsum(
        "ikl,lic->kic", synthesis_mix, grid, preferred_element_type=jnp.float32
    ).astype(jnp.bfloat16)
    conv = jnp.einsum("kij,kjc->kic", synthesis_blocks, spread, preferred_element_type=jnp.float32)
    gated = (gate_out.astype(jnp.float32) * conv.reshape(tokens, chans)).astype(jnp.bfloat16)
    return scatter_sum(gated, out_weight)


def exchange(value, distance):
    pairs = [(source, source ^ distance) for source in range(lax.axis_size("chan"))]
    return lax.ppermute(value, "chan", pairs)


def scatter_sum(gated, out_weight, blocks=4):
    me = lax.axis_index("chan")
    core = me % 2
    chip = me // 2
    width = out_weight.shape[1] // blocks
    pieces = []
    for block in range(blocks):
        pieces.append(scatter_block(gated, out_weight, block, width, core, chip))
    return jnp.concatenate(pieces, axis=1)


def scatter_block(gated, out_weight, block, width, core, chip):
    rows = gated.shape[0]
    weight = out_weight[:, block * width : (block + 1) * width]
    product = jnp.dot(gated, weight, preferred_element_type=jnp.float32)
    quarters = product.reshape(2, 2, rows // 4, width)
    sent = lax.dynamic_index_in_dim(quarters, 1 - core, axis=1, keepdims=False)
    kept = lax.dynamic_index_in_dim(quarters, core, axis=1, keepdims=False)
    half = exchange(sent.astype(jnp.bfloat16), 1)
    other = lax.dynamic_index_in_dim(kept, 1 - chip, axis=0, keepdims=False)
    other = other + lax.dynamic_index_in_dim(half, 1 - chip, axis=0, keepdims=False).astype(jnp.float32)
    quarter = exchange(other.astype(jnp.bfloat16), 2)
    mine = lax.dynamic_index_in_dim(kept, chip, axis=0, keepdims=False)
    mine = mine + lax.dynamic_index_in_dim(half, chip, axis=0, keepdims=False).astype(jnp.float32)
    return (mine + quarter.astype(jnp.float32)).astype(jnp.bfloat16)


def solution(mesh):
    placed = (
        P("seq", "chan"),
        P("seq", "chan"),
        P("seq", "chan"),
        P("seq", "chan"),
        P(),
        P(),
        P(),
        P(),
        P(),
        P("chan", None),
    )
    return jax.shard_map(
        per_device, mesh=mesh, in_specs=placed, out_specs=P(("seq", "chan"), None), check_vma=False
    )
```

```python
import jax
import jax.numpy as jnp
from jax import lax
from jax.experimental import pallas as pl
from jax.experimental.pallas import tpu as pltpu
from jax.sharding import PartitionSpec as P


ROW_SPLIT = 8


def prelude_kernel(gin_ref, vin_ref, filt_ref, blocks_ref, mix_ref, out_ref):
    nb, blk = blocks_ref.shape[0], blocks_ref.shape[1]
    count, rows, lanes = out_ref.shape[0], out_ref.shape[3], out_ref.shape[4]
    cs = count // (blk // rows)
    inner = []
    for k in range(nb):
        part = slice(k * blk, (k + 1) * blk)
        mixed = gin_ref[part, :].astype(jnp.float32) * vin_ref[part, :].astype(jnp.float32)
        inner.append(
            jnp.dot(blocks_ref[k], mixed.astype(jnp.bfloat16), preferred_element_type=jnp.float32)
            .astype(jnp.bfloat16)
            .astype(jnp.float32)
        )
    for k in range(nb):
        acc = mix_ref[:, k * nb : k * nb + 1] * inner[0]
        for l in range(1, nb):
            acc = acc + mix_ref[:, k * nb + l : k * nb + l + 1] * inner[l]
        spec = acc.astype(jnp.bfloat16)
        for a in range(blk // rows):
            for b in range(cs):
                cols = slice(b * lanes, (b + 1) * lanes)
                out_ref[a * cs + b, 0, k] = spec[a * rows : (a + 1) * rows, cols]
                out_ref[a * cs + b, 1, k] = filt_ref[k * blk + a * rows : k * blk + (a + 1) * rows, cols]


def prelude(gate_in, value_in, spectral_filter, blocks, mix, count):
    tokens, chans = gate_in.shape
    nb, blk = blocks.shape[0], blocks.shape[1]
    cs = count // ROW_SPLIT
    vmem = pl.BlockSpec(memory_space=pltpu.VMEM)
    return pl.pallas_call(
        prelude_kernel,
        out_shape=jax.ShapeDtypeStruct((count, 2, nb, blk // ROW_SPLIT, chans // cs), jnp.bfloat16),
        in_specs=[vmem] * 5,
        out_specs=vmem,
        cost_estimate=pl.CostEstimate(
            flops=2 * tokens * blk * chans + 6 * nb * tokens * chans,
            bytes_accessed=2 * 5 * tokens * chans,
            transcendentals=0,
        ),
    )(gate_in, value_in, spectral_filter, blocks, mix.astype(jnp.float32).reshape(blk, nb * nb))


def from_columns(values, count, blk, chans):
    nb = values.shape[1]
    cs = count // ROW_SPLIT
    back = lax.all_to_all(values, "seq", 0, 0, tiled=True)
    back = back.reshape(ROW_SPLIT, cs, nb, blk // ROW_SPLIT, chans // cs)
    return back.transpose(2, 0, 3, 1, 4).reshape(nb, blk, chans)


def rotate_bit(values, cosine, sine, bit, sections, sign):
    axis = sections - 1 - bit
    lower = lax.index_in_dim(values, 0, axis, keepdims=True)
    upper = lax.index_in_dim(values, 1, axis, keepdims=True)
    new_lower = cosine * lower + sign * sine * upper
    new_upper = cosine * upper - sign * sine * lower
    return jnp.concatenate([new_lower, new_upper], axis=axis)


def per_device(
    value_in,
    gate_in,
    gate_out,
    spectral_filter,
    analysis_blocks,
    analysis_mix,
    synthesis_blocks,
    synthesis_mix,
    angles,
    out_weight,
):
    tokens, chans = value_in.shape
    nblocks = analysis_blocks.shape[0]
    blk = analysis_blocks.shape[1]
    count = lax.axis_size("seq")
    sections = count.bit_length() - 1
    rank = lax.axis_index("seq")
    parts = prelude(gate_in, value_in, spectral_filter, analysis_blocks, analysis_mix, count)
    both_cols = lax.all_to_all(parts, "seq", 0, 0, tiled=True)
    spec_cols = both_cols[:, 0]
    filt_cols = both_cols[:, 1]
    rows = blk // ROW_SPLIT
    row_part = rank // (count // ROW_SPLIT)
    theta = angles.reshape(sections, nblocks, ROW_SPLIT, rows)
    theta = lax.dynamic_index_in_dim(theta, row_part, axis=2, keepdims=False)
    cosines = jnp.cos(theta)[:, :, :, None]
    sines = jnp.sin(theta)[:, :, :, None]

    shape = (2,) * sections + spec_cols.shape[1:]
    work = spec_cols.astype(jnp.float32).reshape(shape)
    for section in range(sections):
        work = rotate_bit(work, cosines[section], sines[section], section, sections, 1.0)
    work = work * filt_cols.astype(jnp.float32).reshape(shape)
    for section in reversed(range(sections)):
        work = rotate_bit(work, cosines[section], sines[section], section, sections, -1.0)
    work = work.astype(jnp.bfloat16).reshape(spec_cols.shape)

    grid = from_columns(work, count, blk, chans)
    spread = jnp.einsum(
        "ikl,lic->kic", synthesis_mix, grid, preferred_element_type=jnp.float32
    ).astype(jnp.bfloat16)
    conv = jnp.einsum("kij,kjc->kic", synthesis_blocks, spread, preferred_element_type=jnp.float32)
    gated = (gate_out.astype(jnp.float32) * conv.reshape(tokens, chans)).astype(jnp.bfloat16)
    return scatter_sum(gated, out_weight)


def exchange(value, distance):
    pairs = [(source, source ^ distance) for source in range(lax.axis_size("chan"))]
    return lax.ppermute(value, "chan", pairs)


def scatter_sum(gated, out_weight, blocks=4):
    me = lax.axis_index("chan")
    core = me % 2
    chip = me // 2
    rows, _ = gated.shape
    width = out_weight.shape[1] // blocks
    out = jnp.zeros((rows // 4, out_weight.shape[1]), jnp.bfloat16)
    for block in range(blocks):
        piece = scatter_block(gated, out_weight, block, width, core, chip)
        out = lax.dynamic_update_slice_in_dim(out, piece, block * width, axis=1)
    return out


def scatter_block(gated, out_weight, block, width, core, chip):
    rows = gated.shape[0]
    weight = out_weight[:, block * width : (block + 1) * width]
    product = jnp.dot(gated, weight, preferred_element_type=jnp.float32)
    quarters = product.reshape(2, 2, rows // 4, width)
    sent = lax.dynamic_index_in_dim(quarters, 1 - core, axis=1, keepdims=False)
    kept = lax.dynamic_index_in_dim(quarters, core, axis=1, keepdims=False)
    half = exchange(sent.astype(jnp.bfloat16), 1)
    other = lax.dynamic_index_in_dim(kept, 1 - chip, axis=0, keepdims=False)
    other = other + lax.dynamic_index_in_dim(half, 1 - chip, axis=0, keepdims=False).astype(jnp.float32)
    quarter = exchange(other.astype(jnp.bfloat16), 2)
    mine = lax.dynamic_index_in_dim(kept, chip, axis=0, keepdims=False)
    mine = mine + lax.dynamic_index_in_dim(half, chip, axis=0, keepdims=False).astype(jnp.float32)
    return (mine + quarter.astype(jnp.float32)).astype(jnp.bfloat16)


def solution(mesh):
    placed = (
        P("seq", "chan"),
        P("seq", "chan"),
        P("seq", "chan"),
        P("seq", "chan"),
        P(),
        P(),
        P(),
        P(),
        P(),
        P("chan", None),
    )
    return jax.shard_map(
        per_device, mesh=mesh, in_specs=placed, out_specs=P(("seq", "chan"), None), check_vma=False
    )
```

```python
import jax
import jax.numpy as jnp
from jax import lax
from jax.experimental import pallas as pl
from jax.experimental.pallas import tpu as pltpu
from jax.sharding import PartitionSpec as P


ROW_SPLIT = 8


def prelude_kernel(gin_ref, vin_ref, filt_ref, blocks_ref, mix_ref, out_ref):
    nb, blk = blocks_ref.shape[0], blocks_ref.shape[1]
    count, rows, lanes = out_ref.shape[0], out_ref.shape[3], out_ref.shape[4]
    cs = count // (blk // rows)
    inner = []
    for k in range(nb):
        part = slice(k * blk, (k + 1) * blk)
        mixed = gin_ref[part, :].astype(jnp.float32) * vin_ref[part, :].astype(jnp.float32)
        inner.append(
            jnp.dot(blocks_ref[k], mixed.astype(jnp.bfloat16), preferred_element_type=jnp.float32)
            .astype(jnp.bfloat16)
            .astype(jnp.float32)
        )
    for k in range(nb):
        acc = mix_ref[:, k * nb : k * nb + 1] * inner[0]
        for l in range(1, nb):
            acc = acc + mix_ref[:, k * nb + l : k * nb + l + 1] * inner[l]
        spec = acc.astype(jnp.bfloat16)
        for a in range(blk // rows):
            for b in range(cs):
                cols = slice(b * lanes, (b + 1) * lanes)
                out_ref[a * cs + b, 0, k] = spec[a * rows : (a + 1) * rows, cols]
                out_ref[a * cs + b, 1, k] = filt_ref[k * blk + a * rows : k * blk + (a + 1) * rows, cols]


def prelude(gate_in, value_in, spectral_filter, blocks, mix, count):
    tokens, chans = gate_in.shape
    nb, blk = blocks.shape[0], blocks.shape[1]
    cs = count // ROW_SPLIT
    vmem = pl.BlockSpec(memory_space=pltpu.VMEM)
    return pl.pallas_call(
        prelude_kernel,
        out_shape=jax.ShapeDtypeStruct((count, 2, nb, blk // ROW_SPLIT, chans // cs), jnp.bfloat16),
        in_specs=[vmem] * 5,
        out_specs=vmem,
        cost_estimate=pl.CostEstimate(
            flops=2 * tokens * blk * chans + 6 * nb * tokens * chans,
            bytes_accessed=2 * 5 * tokens * chans,
            transcendentals=0,
        ),
    )(gate_in, value_in, spectral_filter, blocks, mix.astype(jnp.float32).reshape(blk, nb * nb))


def from_columns(values, count, blk, chans):
    nb = values.shape[1]
    cs = count // ROW_SPLIT
    back = lax.all_to_all(values, "seq", 0, 0, tiled=True)
    back = back.reshape(ROW_SPLIT, cs, nb, blk // ROW_SPLIT, chans // cs)
    return back.transpose(2, 0, 3, 1, 4).reshape(nb, blk, chans)


def rotate_bit(values, cosine, sine, bit, sections, sign):
    axis = sections - 1 - bit
    lower = lax.index_in_dim(values, 0, axis, keepdims=True)
    upper = lax.index_in_dim(values, 1, axis, keepdims=True)
    new_lower = cosine * lower + sign * sine * upper
    new_upper = cosine * upper - sign * sine * lower
    return jnp.concatenate([new_lower, new_upper], axis=axis)


def per_device(
    value_in,
    gate_in,
    gate_out,
    spectral_filter,
    analysis_blocks,
    analysis_mix,
    synthesis_blocks,
    synthesis_mix,
    angles,
    out_weight,
):
    tokens, chans = value_in.shape
    nblocks = analysis_blocks.shape[0]
    blk = analysis_blocks.shape[1]
    count = lax.axis_size("seq")
    sections = count.bit_length() - 1
    rank = lax.axis_index("seq")
    parts = prelude(gate_in, value_in, spectral_filter, analysis_blocks, analysis_mix, count)
    both_cols = lax.all_to_all(parts, "seq", 0, 0, tiled=True)
    spec_cols = both_cols[:, 0]
    filt_cols = both_cols[:, 1]
    rows = blk // ROW_SPLIT
    row_part = rank // (count // ROW_SPLIT)
    theta = angles.reshape(sections, nblocks, ROW_SPLIT, rows)
    theta = lax.dynamic_index_in_dim(theta, row_part, axis=2, keepdims=False)
    cosines = jnp.cos(theta)[:, :, :, None]
    sines = jnp.sin(theta)[:, :, :, None]

    shape = (2,) * sections + spec_cols.shape[1:]
    work = spec_cols.astype(jnp.float32).reshape(shape)
    for section in range(sections):
        work = rotate_bit(work, cosines[section], sines[section], section, sections, 1.0)
    work = work * filt_cols.astype(jnp.float32).reshape(shape)
    for section in reversed(range(sections)):
        work = rotate_bit(work, cosines[section], sines[section], section, sections, -1.0)
    work = work.astype(jnp.bfloat16).reshape(spec_cols.shape)

    grid = from_columns(work, count, blk, chans)
    spread = jnp.einsum(
        "ikl,lic->kic", synthesis_mix, grid, preferred_element_type=jnp.float32
    ).astype(jnp.bfloat16)
    conv = jnp.einsum("kij,kjc->kic", synthesis_blocks, spread, preferred_element_type=jnp.float32)
    gated = (gate_out.astype(jnp.float32) * conv.reshape(tokens, chans)).astype(jnp.bfloat16)
    return scatter_sum(gated, out_weight)


def exchange(value, distance):
    pairs = [(source, source ^ distance) for source in range(lax.axis_size("chan"))]
    return lax.ppermute(value, "chan", pairs)


SHARES = (1.5, 1.5, 1.5, 1.5, 2)


def scatter_sum(gated, out_weight, shares=SHARES):
    me = lax.axis_index("chan")
    core = me % 2
    chip = me // 2
    unit = out_weight.shape[1] // 8
    bounds = [0]
    for share in shares:
        bounds.append(bounds[-1] + int(share * unit))
    pieces = []
    for block in range(len(shares)):
        pieces.append(scatter_block(gated, out_weight, bounds[block], bounds[block + 1], core, chip))
    return jnp.concatenate(pieces, axis=1)


def scatter_block(gated, out_weight, start, stop, core, chip):
    rows = gated.shape[0]
    width = stop - start
    weight = out_weight[:, start:stop]
    product = jnp.dot(gated, weight, preferred_element_type=jnp.float32)
    quarters = product.reshape(2, 2, rows // 4, width)
    sent = lax.dynamic_index_in_dim(quarters, 1 - core, axis=1, keepdims=False)
    kept = lax.dynamic_index_in_dim(quarters, core, axis=1, keepdims=False)
    half = exchange(sent.astype(jnp.bfloat16), 1)
    other = lax.dynamic_index_in_dim(kept, 1 - chip, axis=0, keepdims=False)
    other = other + lax.dynamic_index_in_dim(half, 1 - chip, axis=0, keepdims=False).astype(jnp.float32)
    quarter = exchange(other.astype(jnp.bfloat16), 2)
    mine = lax.dynamic_index_in_dim(kept, chip, axis=0, keepdims=False)
    mine = mine + lax.dynamic_index_in_dim(half, chip, axis=0, keepdims=False).astype(jnp.float32)
    return (mine + quarter.astype(jnp.float32)).astype(jnp.bfloat16)


def solution(mesh):
    placed = (
        P("seq", "chan"),
        P("seq", "chan"),
        P("seq", "chan"),
        P("seq", "chan"),
        P(),
        P(),
        P(),
        P(),
        P(),
        P("chan", None),
    )
    return jax.shard_map(
        per_device, mesh=mesh, in_specs=placed, out_specs=P(("seq", "chan"), None), check_vma=False
    )
```
